256 devices in a mesh: chan: 64 (over x, y, z_hi, core), beam: 4 (over z_lo).
Axes of the slice: x: 4, y: 4, z: 8 (z_hi: 2, z_lo: 4; z = z_hi * 4 + z_lo), core: 2. Of those that a mesh axis runs over, the one named last changes fastest.
Arguments:
- images: float32 [256, 36, 128, 128], P('chan', 'beam')
- beam_weight: float32 [36, 128, 128], P('beam'), may hold values from 0.2 to 1
- offsets: int32 [36, 2], P('beam'), may hold values from 0 to 384, as said below
- rejected_indicator: int32 [256, 192, 512], P('chan', None, 'beam'), may hold values 0 or 1
- regression_indicator: int32 [256], replicated, may hold values 0 or 1
Outputs:
- cleaned_cube: float32 [256, 192, 512], P(None, 'chan', 'beam')
The draws below stay inside these ranges and needn't reach their ends.
Inputs may be any that keep to these rules, and one draw needn't show every extreme that they name: `offsets`: beam b = 6 r + q sits near row r * 64 // 5 and column q * 384 // 5, within 16; every sky pixel is covered by some beam; the first and last row and column of beams lie at the field's edges.
All inputs are finite; a program needn't handle non-finite values. No bound on the sum of `rejected_indicator` on one device may be relied on, other than what follows from the above.
Results may differ from the reference program's by a relative error of at most 0.00023.
Values sent between devices are 32-bit elements; how exact they have to be, the bound alone decides.
No kernel may reach another device: no remote copies, remote signals or barrier semaphores. Data moves between devices by JAX's collectives and lax.ppermute only.
A program may use at most 128 MiB of HBM per device.

```python
import jax
import jax.numpy as jnp
from jax import lax

CHANNELS = 256
BEAMS = 36
BSIDE = 128
MOS_ROWS = 192
MOS_COLS = 512


def draw_images(key, part):
    first_key = jax.random.fold_in(key, 101)
    second_key = jax.random.fold_in(key, 202)
    position = (2.0 * jnp.arange(CHANNELS).astype(jnp.float32) + 1.0) / CHANNELS - 1.0
    square = position * position
    shape = (CHANNELS, BEAMS, BSIDE, BSIDE)
    coefficients = jax.random.normal(first_key, (4, BEAMS, BSIDE, BSIDE), jnp.float32)
    noise = jax.random.normal(second_key, shape, jnp.float32)
    scales = (3.0, 1.5, 1.0, 0.7)
    cube = noise + scales[0] * coefficients[0][None]
    cube = cube + scales[1] * position[:, None, None, None] * coefficients[1][None]
    cube = cube + (0.5 * (3.0 * square - 1.0))[:, None, None, None] * coefficients[2][None]
    cube = cube + scales[3] * (0.5 * (5.0 * square * position - 3.0 * position))[:, None, None, None] * coefficients[3][None]
    return cube.astype(jnp.float32)


def draw_offsets(key, part):
    row_key = jax.random.fold_in(key, 303)
    col_key = jax.random.fold_in(key, 404)
    jitter_span = BSIDE // 8
    index = jnp.arange(BEAMS, dtype=jnp.int32)
    grid_row = index // 6
    grid_col = index % 6
    base_row = grid_row * (MOS_ROWS - BSIDE) // 5
    base_col = grid_col * (MOS_COLS - BSIDE) // 5
    row_jitter = jax.random.randint(row_key, (BEAMS,), -jitter_span, jitter_span + 1, jnp.int32)
    col_jitter = jax.random.randint(col_key, (BEAMS,), -jitter_span, jitter_span + 1, jnp.int32)
    row_inner = jnp.logical_and(grid_row > 0, grid_row < 5).astype(jnp.int32)
    col_inner = jnp.logical_and(grid_col > 0, grid_col < 5).astype(jnp.int32)
    row_start = jnp.clip(base_row + row_inner * row_jitter, 0, MOS_ROWS - BSIDE)
    col_start = jnp.clip(base_col + col_inner * col_jitter, 0, MOS_COLS - BSIDE)
    return jnp.stack([row_start, col_start], axis=1).astype(jnp.int32)


def set_ends(values, key, least, largest):
    longest = values.shape.index(max(values.shape))
    spots = []
    for shift in (0, 1):
        where = [jax.random.randint(jax.random.fold_in(key, axis), (), 0, length) for axis, length in enumerate(values.shape)]
        where[longest] = (where[longest] + shift) % values.shape[longest]
        spots.append(tuple(where))
    return values.at[spots[0]].set(least).at[spots[1]].set(largest)


def levels(rng, shape, shards, least, top_value):
    level, own = 1.0, jax.random.fold_in(rng, 6)
    for axis_at, parts in shards:
        draws = jnp.exp(jax.random.uniform(jax.random.fold_in(own, axis_at), (parts,), jnp.float32, least / len(shards), top_value / len(shards)))
        level = level * jnp.repeat(draws, shape[axis_at] // parts).reshape([-1 if axis == axis_at else 1 for axis in range(len(shape))])
    return level


def setup_inputs(seed: int = 0) -> dict:
    keys = jax.random.split(jax.random.key(seed), 6)
    return {
        "images": draw_images(jax.random.fold_in(keys[5], 71), 0),
        "beam_weight": jnp.clip(0.2 + 0.8 * jax.random.uniform(keys[1], (BEAMS, BSIDE, BSIDE), jnp.float32) ** levels(keys[1], (BEAMS, BSIDE, BSIDE), ((0, 4),), -0.2, 0.2), 0.2, 1.0),
        "offsets": draw_offsets(jax.random.fold_in(keys[5], 71), 0),
        "rejected_indicator": set_ends((jax.random.randint(keys[3], (CHANNELS, MOS_ROWS, MOS_COLS), 0, 8) < 1).astype(jnp.int32), jax.random.fold_in(keys[3], 1), 0, 1),
        "regression_indicator": set_ends((jax.random.randint(keys[4], (CHANNELS,), 0, 4) < 3).astype(jnp.int32), jax.random.fold_in(keys[4], 1), 0, 1),
    }


def legendre(count):
    position = (2.0 * jnp.arange(count).astype(jnp.float32) + 1.0) / count - 1.0
    square = position * position
    return jnp.stack([jnp.ones_like(position), position, 0.5 * (3.0 * square - 1.0), 0.5 * (5.0 * square * position - 3.0 * position)], axis=1)

def solve_cubic(normal_matrix, right_side):
    factor = {}
    for outer in range(4):
        for inner in range(outer + 1):
            value = normal_matrix[outer * 4 + inner]
            for other in range(inner):
                value = value - factor[outer, other] * factor[inner, other]
            if outer == inner:
                factor[outer, outer] = jnp.sqrt(value)
            else:
                factor[outer, inner] = value / factor[inner, inner]
    forward = []
    for outer in range(4):
        value = right_side[outer]
        for other in range(outer):
            value = value - factor[outer, other] * forward[other]
        forward.append(value / factor[outer, outer])
    backward = [None] * 4
    for outer in range(3, -1, -1):
        value = forward[outer]
        for other in range(outer + 1, 4):
            value = value - factor[other, outer] * backward[other]
        backward[outer] = value / factor[outer, outer]
    return jnp.stack(backward, axis=0)

def clean_tiles(celestial_image, importance_factor):
    table = legendre(celestial_image.shape[0])
    products = jnp.stack([table[:, outer] * table[:, inner] for outer in range(4) for inner in range(4)], axis=0)
    normal_matrix = jnp.dot(products, importance_factor, precision=lax.Precision.HIGHEST, preferred_element_type=jnp.float32)
    right_side = jnp.dot(table.T, importance_factor * celestial_image, precision=lax.Precision.HIGHEST, preferred_element_type=jnp.float32)
    coefficients = solve_cubic(normal_matrix, right_side)
    continuum = jnp.dot(table, coefficients, precision=lax.Precision.HIGHEST, preferred_element_type=jnp.float32)
    residual = celestial_image - continuum
    padded = jnp.pad(residual, ((1, 1), (0, 0)))
    return 0.25 * padded[:-2] + 0.5 * residual + 0.25 * padded[2:]

def reference(images, beam_weight, offsets, rejected_indicator, regression_indicator):
    exponent = 1.0 + 0.5 * jnp.arange(CHANNELS).astype(jnp.float32) / (CHANNELS - 1)
    side = images.shape[2]

    def place(index, state_pair):
        dividend_accumulator, normalizer_accumulated = state_pair
        beam_image = lax.dynamic_index_in_dim(images, index, 1, keepdims=False)
        log_weight = jnp.log(lax.dynamic_index_in_dim(beam_weight, index, 0, keepdims=False))
        response = jnp.exp(exponent[:, None, None] * log_weight[None])
        corner = (jnp.zeros((), jnp.int32), offsets[index, 0].astype(jnp.int32), offsets[index, 1].astype(jnp.int32))
        extent = (CHANNELS, side, side)
        dividend_accumulator = lax.dynamic_update_slice(dividend_accumulator, lax.dynamic_slice(dividend_accumulator, corner, extent) + response * beam_image, corner)
        normalizer_accumulated = lax.dynamic_update_slice(normalizer_accumulated, lax.dynamic_slice(normalizer_accumulated, corner, extent) + response * response, corner)
        return (dividend_accumulator, normalizer_accumulated)
    empty = jnp.zeros((CHANNELS, MOS_ROWS, MOS_COLS), jnp.float32)
    dividend_accumulator, normalizer_accumulated = lax.fori_loop(0, BEAMS, place, (empty, empty))
    accepted_entries = 1.0 - rejected_indicator.astype(jnp.float32)
    celestial_image = accepted_entries * dividend_accumulator / normalizer_accumulated
    importance_factor = normalizer_accumulated * (regression_indicator.astype(jnp.float32)[:, None, None] * accepted_entries + 0.01)
    flat_sky = celestial_image.reshape(CHANNELS, MOS_ROWS * MOS_COLS)
    flat_weight = importance_factor.reshape(CHANNELS, MOS_ROWS * MOS_COLS)
    return clean_tiles(flat_sky, flat_weight).reshape(CHANNELS, MOS_ROWS, MOS_COLS)
```

```python
import jax
import jax.numpy as jnp
from jax import lax
from jax.sharding import PartitionSpec as P

MOS_ROWS = 192
MOS_COLS = 512


def legendre(count):
    position = (2.0 * jnp.arange(count).astype(jnp.float32) + 1.0) / count - 1.0
    square = position * position
    return jnp.stack(
        [
            jnp.ones_like(position),
            position,
            0.5 * (3.0 * square - 1.0),
            0.5 * (5.0 * square * position - 3.0 * position),
        ],
        axis=1,
    )


def solve_cubic(normal_matrix, right_side):
    factor = {}
    for outer in range(4):
        for inner in range(outer + 1):
            value = normal_matrix[outer * 4 + inner]
            for other in range(inner):
                value = value - factor[outer, other] * factor[inner, other]
            if outer == inner:
                factor[outer, outer] = jnp.sqrt(value)
            else:
                factor[outer, inner] = value / factor[inner, inner]
    forward = []
    for outer in range(4):
        value = right_side[outer]
        for other in range(outer):
            value = value - factor[outer, other] * forward[other]
        forward.append(value / factor[outer, outer])
    backward = [None] * 4
    for outer in range(3, -1, -1):
        value = forward[outer]
        for other in range(outer + 1, 4):
            value = value - factor[other, outer] * backward[other]
        backward[outer] = value / factor[outer, outer]
    return jnp.stack(backward, axis=0)


def clean_pair(pair):
    sky_tile, weight_tile = pair
    channels, rows, columns = sky_tile.shape
    celestial_image = sky_tile.reshape(channels, rows * columns)
    importance_factor = weight_tile.reshape(channels, rows * columns)
    table = legendre(channels)
    products = jnp.stack(
        [table[:, outer] * table[:, inner] for outer in range(4) for inner in range(4)], axis=0
    )
    normal_matrix = jnp.dot(
        products,
        importance_factor,
        precision=lax.Precision.HIGHEST,
        preferred_element_type=jnp.float32,
    )
    right_side = jnp.dot(
        table.T,
        importance_factor * celestial_image,
        precision=lax.Precision.HIGHEST,
        preferred_element_type=jnp.float32,
    )
    coefficients = solve_cubic(normal_matrix, right_side)
    continuum = jnp.dot(
        table, coefficients, precision=lax.Precision.HIGHEST, preferred_element_type=jnp.float32
    )
    residual = celestial_image - continuum
    padded = jnp.pad(residual, ((1, 1), (0, 0)))
    smoothed = 0.25 * padded[:-2] + 0.5 * residual + 0.25 * padded[2:]
    return smoothed.reshape(channels, rows, columns)


def local(images, beam_weight, offsets, rejected_indicator, regression_indicator):
    ch_dev = images.shape[0]
    side = images.shape[2]
    all_channels = regression_indicator.shape[0]
    first_channel = lax.axis_index("chan") * ch_dev
    channel_ids = first_channel + jnp.arange(ch_dev, dtype=jnp.int32)
    exponent = 1.0 + 0.5 * channel_ids.astype(jnp.float32) / (all_channels - 1)
    log_weight = jnp.log(beam_weight)
    response = jnp.exp(exponent[:, None, None, None] * log_weight[None])
    stacked = jnp.stack([response * images, response * response])
    row_hit = (
        lax.broadcasted_iota(jnp.int32, (1, MOS_ROWS, side), 1)
        == lax.broadcasted_iota(jnp.int32, (1, MOS_ROWS, side), 2) + offsets[:, 0, None, None]
    ).astype(jnp.float32)
    col_hit = (
        lax.broadcasted_iota(jnp.int32, (1, side, MOS_COLS), 2)
        == lax.broadcasted_iota(jnp.int32, (1, side, MOS_COLS), 1) + offsets[:, 1, None, None]
    ).astype(jnp.float32)
    rows_placed = jnp.einsum(
        "bri,acbij->bacrj", row_hit, stacked, precision=lax.Precision.HIGHEST,
        preferred_element_type=jnp.float32,
    )
    planes = jnp.einsum(
        "bacrj,bjk->acrk", rows_placed, col_hit, precision=lax.Precision.HIGHEST,
        preferred_element_type=jnp.float32,
    )
    own = lax.psum_scatter(planes, "beam", scatter_dimension=3, tiled=True)
    dividend_accumulator = own[0]
    normalizer_accumulated = own[1]
    accepted_entries = 1.0 - rejected_indicator.astype(jnp.float32)
    emission_absent = lax.dynamic_slice_in_dim(regression_indicator, first_channel, ch_dev).astype(
        jnp.float32
    )
    celestial_image = accepted_entries * dividend_accumulator / normalizer_accumulated
    importance_factor = normalizer_accumulated * (
        emission_absent[:, None, None] * accepted_entries + 0.01
    )
    arrived = lax.all_to_all(
        jnp.stack([celestial_image, importance_factor]), "chan", split_axis=2, concat_axis=1, tiled=True
    )
    return clean_pair((arrived[0], arrived[1]))


def solution(mesh):
    in_specs = (
        P("chan", "beam", None, None),
        P("beam", None, None),
        P("beam", None),
        P("chan", None, "beam"),
        P(),
    )
    out_specs = P(None, "chan", "beam")
    return jax.shard_map(local, mesh=mesh, in_specs=in_specs, out_specs=out_specs, check_vma=False)
```

```python
import jax
import jax.numpy as jnp
from jax import lax
from jax.sharding import PartitionSpec as P


MOS_ROWS = 192
MOS_COLS = 512


def legendre(count):
    position = (2.0 * jnp.arange(count).astype(jnp.float32) + 1.0) / count - 1.0
    square = position * position
    return jnp.stack(
        [
            jnp.ones_like(position),
            position,
            0.5 * (3.0 * square - 1.0),
            0.5 * (5.0 * square * position - 3.0 * position),
        ],
        axis=1,
    )


def solve_cubic(normal_matrix, right_side):
    factor = {}
    for outer in range(4):
        for inner in range(outer + 1):
            value = normal_matrix[outer * 4 + inner]
            for other in range(inner):
                value = value - factor[outer, other] * factor[inner, other]
            if outer == inner:
                factor[outer, outer] = jnp.sqrt(value)
            else:
                factor[outer, inner] = value / factor[inner, inner]
    forward = []
    for outer in range(4):
        value = right_side[outer]
        for other in range(outer):
            value = value - factor[outer, other] * forward[other]
        forward.append(value / factor[outer, outer])
    backward = [None] * 4
    for outer in range(3, -1, -1):
        value = forward[outer]
        for other in range(outer + 1, 4):
            value = value - factor[other, outer] * backward[other]
        backward[outer] = value / factor[outer, outer]
    return jnp.stack(backward, axis=0)


def clean_pair(pair):
    sky_tile, weight_tile = pair
    channels, rows, columns = sky_tile.shape
    celestial_image = sky_tile.reshape(channels, rows * columns)
    importance_factor = weight_tile.reshape(channels, rows * columns)
    table = legendre(channels)
    products = jnp.stack(
        [table[:, outer] * table[:, inner] for outer in range(4) for inner in range(4)], axis=0
    )
    normal_matrix = jnp.dot(
        products,
        importance_factor,
        precision=lax.Precision.HIGHEST,
        preferred_element_type=jnp.float32,
    )
    right_side = jnp.dot(
        table.T,
        importance_factor * celestial_image,
        precision=lax.Precision.HIGHEST,
        preferred_element_type=jnp.float32,
    )
    coefficients = solve_cubic(normal_matrix, right_side)
    continuum = jnp.dot(
        table, coefficients, precision=lax.Precision.HIGHEST, preferred_element_type=jnp.float32
    )
    residual = celestial_image - continuum
    padded = jnp.pad(residual, ((1, 1), (0, 0)))
    smoothed = 0.25 * padded[:-2] + 0.5 * residual + 0.25 * padded[2:]
    return smoothed.reshape(channels, rows, columns)


CHUNKS = 2


def place_and_reduce(images, log_weight, offsets, exponent, rejected, emission_absent):
    side = images.shape[2]
    response = jnp.exp(exponent[:, None, None, None] * log_weight[None])
    stacked = jnp.stack([response * images, response * response])
    row_hit = (
        lax.broadcasted_iota(jnp.int32, (1, MOS_ROWS, side), 1)
        == lax.broadcasted_iota(jnp.int32, (1, MOS_ROWS, side), 2) + offsets[:, 0, None, None]
    ).astype(jnp.float32)
    col_hit = (
        lax.broadcasted_iota(jnp.int32, (1, side, MOS_COLS), 2)
        == lax.broadcasted_iota(jnp.int32, (1, side, MOS_COLS), 1) + offsets[:, 1, None, None]
    ).astype(jnp.float32)
    rows_placed = jnp.einsum(
        "bri,acbij->bacrj", row_hit, stacked, precision=lax.Precision.HIGHEST,
        preferred_element_type=jnp.float32,
    )
    planes = jnp.einsum(
        "bacrj,bjk->acrk", rows_placed, col_hit, precision=lax.Precision.HIGHEST,
        preferred_element_type=jnp.float32,
    )
    own = lax.psum_scatter(planes, "beam", scatter_dimension=3, tiled=True)
    own, rejected, emission_absent = lax.optimization_barrier((own, rejected, emission_absent))
    dividend_accumulator = own[0]
    normalizer_accumulated = own[1]
    accepted_entries = 1.0 - rejected.astype(jnp.float32)
    celestial_image = accepted_entries * dividend_accumulator / normalizer_accumulated
    importance_factor = normalizer_accumulated * (
        emission_absent[:, None, None] * accepted_entries + 0.01
    )
    return lax.all_to_all(
        jnp.stack([celestial_image, importance_factor]), "chan", split_axis=2, concat_axis=1,
        tiled=True,
    )


def local_body(images, beam_weight, offsets, rejected_indicator, regression_indicator):
    ch_dev = images.shape[0]
    all_channels = regression_indicator.shape[0]
    first_channel = lax.axis_index("chan") * ch_dev
    channel_ids = first_channel + jnp.arange(ch_dev, dtype=jnp.int32)
    exponent = 1.0 + 0.5 * channel_ids.astype(jnp.float32) / (all_channels - 1)
    emission_absent = lax.dynamic_slice_in_dim(regression_indicator, first_channel, ch_dev).astype(
        jnp.float32
    )
    log_weight = jnp.log(beam_weight)
    per_chunk = ch_dev // CHUNKS
    parts = []
    for chunk in range(CHUNKS):
        window = slice(chunk * per_chunk, (chunk + 1) * per_chunk)
        parts.append(
            place_and_reduce(
                images[window], log_weight, offsets, exponent[window],
                rejected_indicator[window], emission_absent[window],
            )
        )
    sources = all_channels // ch_dev
    rows = parts[0].shape[2]
    gathered = jnp.stack(
        [part.reshape(2, sources, per_chunk, rows, -1) for part in parts], axis=2
    ).reshape(2, all_channels, rows, -1)
    return clean_pair((gathered[0], gathered[1]))


def solution(mesh):
    in_specs = (
        P("chan", "beam", None, None),
        P("beam", None, None),
        P("beam", None),
        P("chan", None, "beam"),
        P(),
    )
    out_specs = P(None, "chan", "beam")
    return jax.shard_map(local_body, mesh=mesh, in_specs=in_specs, out_specs=out_specs, check_vma=False)
```

```python
import jax
import jax.numpy as jnp
from jax import lax
from jax.sharding import PartitionSpec as P

MOS_ROWS = 192
MOS_COLS = 512


def legendre(count):
    position = (2.0 * jnp.arange(count).astype(jnp.float32) + 1.0) / count - 1.0
    square = position * position
    return jnp.stack(
        [
            jnp.ones_like(position),
            position,
            0.5 * (3.0 * square - 1.0),
            0.5 * (5.0 * square * position - 3.0 * position),
        ],
        axis=1,
    )


def solve_cubic(normal_matrix, right_side):
    factor = {}
    for outer in range(4):
        for inner in range(outer + 1):
            value = normal_matrix[outer * 4 + inner]
            for other in range(inner):
                value = value - factor[outer, other] * factor[inner, other]
            if outer == inner:
                factor[outer, outer] = jnp.sqrt(value)
            else:
                factor[outer, inner] = value / factor[inner, inner]
    forward = []
    for outer in range(4):
        value = right_side[outer]
        for other in range(outer):
            value = value - factor[outer, other] * forward[other]
        forward.append(value / factor[outer, outer])
    backward = [None] * 4
    for outer in range(3, -1, -1):
        value = forward[outer]
        for other in range(outer + 1, 4):
            value = value - factor[other, outer] * backward[other]
        backward[outer] = value / factor[outer, outer]
    return jnp.stack(backward, axis=0)


def clean_pair(pair):
    sky_tile, weight_tile = pair
    channels, rows, columns = sky_tile.shape
    celestial_image = sky_tile.reshape(channels, rows * columns)
    importance_factor = weight_tile.reshape(channels, rows * columns)
    table = legendre(channels)
    products = jnp.stack(
        [table[:, outer] * table[:, inner] for outer in range(4) for inner in range(4)], axis=0
    )
    normal_matrix = jnp.dot(
        products,
        importance_factor,
        precision=lax.Precision.HIGHEST,
        preferred_element_type=jnp.float32,
    )
    right_side = jnp.dot(
        table.T,
        importance_factor * celestial_image,
        precision=lax.Precision.HIGHEST,
        preferred_element_type=jnp.float32,
    )
    coefficients = solve_cubic(normal_matrix, right_side)
    continuum = jnp.dot(
        table, coefficients, precision=lax.Precision.HIGHEST, preferred_element_type=jnp.float32
    )
    residual = celestial_image - continuum
    padded = jnp.pad(residual, ((1, 1), (0, 0)))
    smoothed = 0.25 * padded[:-2] + 0.5 * residual + 0.25 * padded[2:]
    return smoothed.reshape(channels, rows, columns)


def local(images, beam_weight, offsets, rejected_indicator, regression_indicator):
    ch_dev = images.shape[0]
    side = images.shape[2]
    all_channels = regression_indicator.shape[0]
    first_channel = lax.axis_index("chan") * ch_dev
    channel_ids = first_channel + jnp.arange(ch_dev, dtype=jnp.int32)
    exponent = 1.0 + 0.5 * channel_ids.astype(jnp.float32) / (all_channels - 1)
    log_weight = jnp.log(beam_weight)
    response = jnp.exp(exponent[:, None, None, None] * log_weight[None])
    stacked = jnp.stack([response * images, response * response])
    high = lax.reduce_precision(stacked, exponent_bits=8, mantissa_bits=7)
    rest = stacked - high
    middle = lax.reduce_precision(rest, exponent_bits=8, mantissa_bits=7)
    low = rest - middle
    pieces = jnp.stack([high, middle, low]).astype(jnp.bfloat16)
    row_hit = (
        lax.broadcasted_iota(jnp.int32, (1, MOS_ROWS, side), 1)
        == lax.broadcasted_iota(jnp.int32, (1, MOS_ROWS, side), 2) + offsets[:, 0, None, None]
    ).astype(jnp.bfloat16)
    col_hit = (
        lax.broadcasted_iota(jnp.int32, (1, 1, side, MOS_COLS), 3)
        == lax.broadcasted_iota(jnp.int32, (1, 1, side, MOS_COLS), 2) + offsets[:, 1, None, None, None]
    ).astype(jnp.bfloat16)
    col_hit = jnp.broadcast_to(col_hit, (col_hit.shape[0], 3, side, MOS_COLS))
    rows_placed = jnp.einsum(
        "bri,pacbij->bpacrj", row_hit, pieces, preferred_element_type=jnp.bfloat16
    )
    planes = jnp.einsum(
        "bpacrj,bpjk->acrk", rows_placed, col_hit, preferred_element_type=jnp.float32
    )
    own = lax.psum_scatter(planes, "beam", scatter_dimension=3, tiled=True)
    dividend_accumulator = own[0]
    normalizer_accumulated = own[1]
    accepted_entries = 1.0 - rejected_indicator.astype(jnp.float32)
    emission_absent = lax.dynamic_slice_in_dim(regression_indicator, first_channel, ch_dev).astype(
        jnp.float32
    )
    celestial_image = accepted_entries * dividend_accumulator / normalizer_accumulated
    importance_factor = normalizer_accumulated * (
        emission_absent[:, None, None] * accepted_entries + 0.01
    )
    arrived = lax.all_to_all(
        jnp.stack([celestial_image, importance_factor]), "chan", split_axis=2, concat_axis=1, tiled=True
    )
    return clean_pair((arrived[0], arrived[1]))


def solution(mesh):
    in_specs = (
        P("chan", "beam", None, None),
        P("beam", None, None),
        P("beam", None),
        P("chan", None, "beam"),
        P(),
    )
    out_specs = P(None, "chan", "beam")
    return jax.shard_map(local, mesh=mesh, in_specs=in_specs, out_specs=out_specs, check_vma=False)
```

```python
import jax
import jax.numpy as jnp
from jax import lax
from jax.sharding import PartitionSpec as P

MOS_ROWS = 192
CHAN = ("xy", "zhi", "core")
MOS_COLS = 512


def legendre(count):
    position = (2.0 * jnp.arange(count).astype(jnp.float32) + 1.0) / count - 1.0
    square = position * position
    return jnp.stack(
        [
            jnp.ones_like(position),
            position,
            0.5 * (3.0 * square - 1.0),
            0.5 * (5.0 * square * position - 3.0 * position),
        ],
        axis=1,
    )


def solve_cubic(normal_matrix, right_side):
    factor = {}
    for outer in range(4):
        for inner in range(outer + 1):
            value = normal_matrix[outer * 4 + inner]
            for other in range(inner):
                value = value - factor[outer, other] * factor[inner, other]
            if outer == inner:
                factor[outer, outer] = jnp.sqrt(value)
            else:
                factor[outer, inner] = value / factor[inner, inner]
    forward = []
    for outer in range(4):
        value = right_side[outer]
        for other in range(outer):
            value = value - factor[outer, other] * forward[other]
        forward.append(value / factor[outer, outer])
    backward = [None] * 4
    for outer in range(3, -1, -1):
        value = forward[outer]
        for other in range(outer + 1, 4):
            value = value - factor[other, outer] * backward[other]
        backward[outer] = value / factor[outer, outer]
    return jnp.stack(backward, axis=0)


def clean_pair(pair):
    sky_tile, weight_tile = pair
    channels, rows, columns = sky_tile.shape
    celestial_image = sky_tile.reshape(channels, rows * columns)
    importance_factor = weight_tile.reshape(channels, rows * columns)
    table = legendre(channels)
    products = jnp.stack(
        [table[:, outer] * table[:, inner] for outer in range(4) for inner in range(4)], axis=0
    )
    normal_matrix = jnp.dot(
        products,
        importance_factor,
        precision=lax.Precision.HIGHEST,
        preferred_element_type=jnp.float32,
    )
    right_side = jnp.dot(
        table.T,
        importance_factor * celestial_image,
        precision=lax.Precision.HIGHEST,
        preferred_element_type=jnp.float32,
    )
    coefficients = solve_cubic(normal_matrix, right_side)
    continuum = jnp.dot(
        table, coefficients, precision=lax.Precision.HIGHEST, preferred_element_type=jnp.float32
    )
    residual = celestial_image - continuum
    padded = jnp.pad(residual, ((1, 1), (0, 0)))
    smoothed = 0.25 * padded[:-2] + 0.5 * residual + 0.25 * padded[2:]
    return smoothed.reshape(channels, rows, columns)


def local(images, beam_weight, offsets, rejected_indicator, regression_indicator):
    ch_dev = images.shape[0]
    side = images.shape[2]
    all_channels = regression_indicator.shape[0]
    first_channel = lax.axis_index(CHAN) * ch_dev
    channel_ids = first_channel + jnp.arange(ch_dev, dtype=jnp.int32)
    exponent = 1.0 + 0.5 * channel_ids.astype(jnp.float32) / (all_channels - 1)
    log_weight = jnp.log(beam_weight)
    response = jnp.exp(exponent[:, None, None, None] * log_weight[None])
    stacked = jnp.stack([response * images, response * response])
    row_hit = (
        lax.broadcasted_iota(jnp.int32, (1, MOS_ROWS, side), 1)
        == lax.broadcasted_iota(jnp.int32, (1, MOS_ROWS, side), 2) + offsets[:, 0, None, None]
    ).astype(jnp.float32)
    col_hit = (
        lax.broadcasted_iota(jnp.int32, (1, side, MOS_COLS), 2)
        == lax.broadcasted_iota(jnp.int32, (1, side, MOS_COLS), 1) + offsets[:, 1, None, None]
    ).astype(jnp.float32)
    rows_placed = jnp.einsum(
        "bri,acbij->bacrj", row_hit, stacked, precision=lax.Precision.HIGHEST,
        preferred_element_type=jnp.float32,
    )
    planes = jnp.einsum(
        "bacrj,bjk->acrk", rows_placed, col_hit, precision=lax.Precision.HIGHEST,
        preferred_element_type=jnp.float32,
    )
    own = lax.psum_scatter(planes, "beam", scatter_dimension=3, tiled=True)
    dividend_accumulator = own[0]
    normalizer_accumulated = own[1]
    accepted_entries = 1.0 - rejected_indicator.astype(jnp.float32)
    emission_absent = lax.dynamic_slice_in_dim(regression_indicator, first_channel, ch_dev).astype(
        jnp.float32
    )
    celestial_image = accepted_entries * dividend_accumulator / normalizer_accumulated
    importance_factor = normalizer_accumulated * (
        emission_absent[:, None, None] * accepted_entries + 0.01
    )
    both = jnp.stack([celestial_image, importance_factor])
    col_dev = both.shape[3]
    planes_xy = lax.psum(1, "xy")
    planes_zc = lax.psum(1, ("zhi", "core"))
    rows_dev = both.shape[2] // (planes_xy * planes_zc)
    both = both.reshape(2, ch_dev, planes_xy, planes_zc * rows_dev, col_dev)
    both = lax.all_to_all(both, "xy", split_axis=2, concat_axis=2, tiled=True)
    both = lax.all_to_all(both, ("zhi", "core"), split_axis=3, concat_axis=3, tiled=True)
    both = both.reshape(2, ch_dev, planes_xy, planes_zc, rows_dev, col_dev)
    both = both.transpose(0, 2, 3, 1, 4, 5).reshape(2, all_channels, rows_dev, col_dev)
    return clean_pair((both[0], both[1]))


def solution(mesh):
    devices = mesh.devices
    planes = devices.shape[0] // 4
    split = jax.sharding.Mesh(devices.reshape(planes, 2, 2, devices.shape[1]), ("xy", "zhi", "core", "beam"))
    in_specs = (
        P(CHAN, "beam", None, None),
        P("beam", None, None),
        P("beam", None),
        P(CHAN, None, "beam"),
        P(),
    )
    out_specs = P(None, CHAN, "beam")
    return jax.shard_map(local, mesh=split, in_specs=in_specs, out_specs=out_specs, check_vma=False)
```

```python
import jax
import jax.numpy as jnp
from jax import lax
from jax.sharding import PartitionSpec as P


MOS_ROWS = 192
MOS_COLS = 512


def legendre(count):
    position = (2.0 * jnp.arange(count).astype(jnp.float32) + 1.0) / count - 1.0
    square = position * position
    return jnp.stack(
        [
            jnp.ones_like(position),
            position,
            0.5 * (3.0 * square - 1.0),
            0.5 * (5.0 * square * position - 3.0 * position),
        ],
        axis=1,
    )


def solve_cubic(normal_matrix, right_side):
    factor = {}
    for outer in range(4):
        for inner in range(outer + 1):
            value = normal_matrix[outer * 4 + inner]
            for other in range(inner):
                value = value - factor[outer, other] * factor[inner, other]
            if outer == inner:
                factor[outer, outer] = jnp.sqrt(value)
            else:
                factor[outer, inner] = value / factor[inner, inner]
    forward = []
    for outer in range(4):
        value = right_side[outer]
        for other in range(outer):
            value = value - factor[outer, other] * forward[other]
        forward.append(value / factor[outer, outer])
    backward = [None] * 4
    for outer in range(3, -1, -1):
        value = forward[outer]
        for other in range(outer + 1, 4):
            value = value - factor[other, outer] * backward[other]
        backward[outer] = value / factor[outer, outer]
    return jnp.stack(backward, axis=0)


def clean_pair(pair):
    sky_tile, weight_tile = pair
    channels, rows, columns = sky_tile.shape
    celestial_image = sky_tile.reshape(channels, rows * columns)
    importance_factor = weight_tile.reshape(channels, rows * columns)
    table = legendre(channels)
    products = jnp.stack(
        [table[:, outer] * table[:, inner] for outer in range(4) for inner in range(4)], axis=0
    )
    normal_matrix = jnp.dot(
        products,
        importance_factor,
        precision=lax.Precision.HIGHEST,
        preferred_element_type=jnp.float32,
    )
    right_side = jnp.dot(
        table.T,
        importance_factor * celestial_image,
        precision=lax.Precision.HIGHEST,
        preferred_element_type=jnp.float32,
    )
    coefficients = solve_cubic(normal_matrix, right_side)
    continuum = jnp.dot(
        table, coefficients, precision=lax.Precision.HIGHEST, preferred_element_type=jnp.float32
    )
    residual = celestial_image - continuum
    padded = jnp.pad(residual, ((1, 1), (0, 0)))
    smoothed = 0.25 * padded[:-2] + 0.5 * residual + 0.25 * padded[2:]
    return smoothed.reshape(channels, rows, columns)


JITTER = 16


def covered_rows(groups, per_group, side):
    grid = int(round((groups * per_group) ** 0.5))
    block = MOS_COLS // groups

    def span(base, inner, top):
        return (max(base - JITTER, 0), min(base + JITTER, top)) if inner else (base, base)

    cover = {}
    for group in range(groups):
        for target in range(groups):
            rows = None
            for index in range(per_group):
                beam = group * per_group + index
                row, col = beam // grid, beam % grid
                row_lo, row_hi = span(row * (MOS_ROWS - side) // (grid - 1), 0 < row < grid - 1, MOS_ROWS - side)
                col_lo, col_hi = span(col * (MOS_COLS - side) // (grid - 1), 0 < col < grid - 1, MOS_COLS - side)
                if col_lo < block * (target + 1) and col_hi + side > block * target:
                    low, high = row_lo, row_hi + side
                    rows = (low, high) if rows is None else (min(rows[0], low), max(rows[1], high))
            cover[group, target] = rows
    return cover


def join(first, second):
    if first is None:
        return second
    if second is None:
        return first
    return (min(first[0], second[0]), max(first[1], second[1]))


def step_windows(cover, groups, rightward):
    windows = []
    for step in range(1, groups):
        window = None
        senders = range(step) if rightward else range(groups - step, groups)
        for sender in senders:
            target = sender + groups - step if rightward else sender - groups + step
            contributors = range(sender + 1) if rightward else range(sender, groups)
            for contributor in contributors:
                window = join(window, cover[contributor, target])
        low = (window[0] // 8) * 8
        high = min(-(-window[1] // 8) * 8, MOS_ROWS)
        windows.append((low, high))
    return windows


def line_reduce_scatter(planes, per_group, side):
    groups = lax.psum(1, "beam")
    block = MOS_COLS // groups
    me = lax.axis_index("beam")
    cover = covered_rows(groups, per_group, side)
    total = lax.dynamic_slice_in_dim(planes, me * block, block, 3)
    for rightward in (True, False):
        windows = step_windows(cover, groups, rightward)
        carried = None
        for step, (low, high) in enumerate(windows, start=1):
            target = me + groups - step if rightward else me - groups + step
            target = jnp.clip(target, 0, groups - 1)
            piece = lax.dynamic_slice(
                planes, (0, 0, low, target * block), planes.shape[:2] + (high - low, block)
            )
            if carried is not None:
                before_low, before_high = windows[step - 2]
                piece = piece.at[:, :, before_low - low : before_high - low].add(carried)
            pairs = (
                [(i, i + 1) for i in range(step)]
                if rightward
                else [(i, i - 1) for i in range(groups - step, groups)]
            )
            carried = lax.ppermute(piece, "beam", pairs)
        low, high = windows[-1]
        total = total.at[:, :, low:high].add(carried)
    return total


def local_body(images, beam_weight, offsets, rejected_indicator, regression_indicator):
    ch_dev = images.shape[0]
    side = images.shape[2]
    all_channels = regression_indicator.shape[0]
    first_channel = lax.axis_index("chan") * ch_dev
    channel_ids = first_channel + jnp.arange(ch_dev, dtype=jnp.int32)
    exponent = 1.0 + 0.5 * channel_ids.astype(jnp.float32) / (all_channels - 1)
    log_weight = jnp.log(beam_weight)
    response = jnp.exp(exponent[:, None, None, None] * log_weight[None])
    stacked = jnp.stack([response * images, response * response])
    side_rows = MOS_ROWS - side
    side_cols = MOS_COLS - side
    row_start = jnp.clip(offsets[:, 0], 0, side_rows)
    col_start = jnp.clip(offsets[:, 1], 0, side_cols)
    row_hit = (
        lax.broadcasted_iota(jnp.int32, (1, MOS_ROWS, side), 1)
        == lax.broadcasted_iota(jnp.int32, (1, MOS_ROWS, side), 2) + row_start[:, None, None]
    ).astype(jnp.float32)
    col_hit = (
        lax.broadcasted_iota(jnp.int32, (1, side, MOS_COLS), 2)
        == lax.broadcasted_iota(jnp.int32, (1, side, MOS_COLS), 1) + col_start[:, None, None]
    ).astype(jnp.float32)
    rows_placed = jnp.einsum(
        "bri,acbij->bacrj", row_hit, stacked, precision=lax.Precision.HIGHEST,
        preferred_element_type=jnp.float32,
    )
    planes = jnp.einsum(
        "bacrj,bjk->acrk", rows_placed, col_hit, precision=lax.Precision.HIGHEST,
        preferred_element_type=jnp.float32,
    )
    own = line_reduce_scatter(planes, images.shape[1], side)
    dividend_accumulator = own[0]
    normalizer_accumulated = own[1]
    accepted_entries = 1.0 - rejected_indicator.astype(jnp.float32)
    emission_absent = lax.dynamic_slice_in_dim(regression_indicator, first_channel, ch_dev).astype(
        jnp.float32
    )
    celestial_image = accepted_entries * dividend_accumulator / normalizer_accumulated
    importance_factor = normalizer_accumulated * (
        emission_absent[:, None, None] * accepted_entries + 0.01
    )
    arrived = lax.all_to_all(
        jnp.stack([celestial_image, importance_factor]), "chan", split_axis=2, concat_axis=1, tiled=True
    )
    return clean_pair((arrived[0], arrived[1]))


def solution(mesh):
    in_specs = (
        P("chan", "beam", None, None),
        P("beam", None, None),
        P("beam", None),
        P("chan", None, "beam"),
        P(),
    )
    out_specs = P(None, "chan", "beam")
    return jax.shard_map(local_body, mesh=mesh, in_specs=in_specs, out_specs=out_specs, check_vma=False)
```

```python
import jax
import jax.numpy as jnp
from jax import lax
from jax.sharding import PartitionSpec as P

MOS_ROWS = 192
MOS_COLS = 512


def legendre(count):
    position = (2.0 * jnp.arange(count).astype(jnp.float32) + 1.0) / count - 1.0
    square = position * position
    return jnp.stack(
        [
            jnp.ones_like(position),
            position,
            0.5 * (3.0 * square - 1.0),
            0.5 * (5.0 * square * position - 3.0 * position),
        ],
        axis=1,
    )


def solve_cubic(normal_matrix, right_side):
    factor = {}
    for outer in range(4):
        for inner in range(outer + 1):
            value = normal_matrix[outer * 4 + inner]
            for other in range(inner):
                value = value - factor[outer, other] * factor[inner, other]
            if outer == inner:
                factor[outer, outer] = jnp.sqrt(value)
            else:
                factor[outer, inner] = value / factor[inner, inner]
    forward = []
    for outer in range(4):
        value = right_side[outer]
        for other in range(outer):
            value = value - factor[outer, other] * forward[other]
        forward.append(value / factor[outer, outer])
    backward = [None] * 4
    for outer in range(3, -1, -1):
        value = forward[outer]
        for other in range(outer + 1, 4):
            value = value - factor[other, outer] * backward[other]
        backward[outer] = value / factor[outer, outer]
    return jnp.stack(backward, axis=0)


def clean_pair(pair):
    sky_tile, weight_tile = pair
    channels, rows, columns = sky_tile.shape
    celestial_image = sky_tile.reshape(channels, rows * columns)
    importance_factor = weight_tile.reshape(channels, rows * columns)
    table = legendre(channels)
    products = jnp.stack(
        [table[:, outer] * table[:, inner] for outer in range(4) for inner in range(4)], axis=0
    )
    normal_matrix = jnp.dot(
        products,
        importance_factor,
        precision=lax.Precision.HIGHEST,
        preferred_element_type=jnp.float32,
    )
    right_side = jnp.dot(
        table.T,
        importance_factor * celestial_image,
        precision=lax.Precision.HIGHEST,
        preferred_element_type=jnp.float32,
    )
    coefficients = solve_cubic(normal_matrix, right_side)
    continuum = jnp.dot(
        table, coefficients, precision=lax.Precision.HIGHEST, preferred_element_type=jnp.float32
    )
    residual = celestial_image - continuum
    padded = jnp.pad(residual, ((1, 1), (0, 0)))
    smoothed = 0.25 * padded[:-2] + 0.5 * residual + 0.25 * padded[2:]
    return smoothed.reshape(channels, rows, columns)


def place(values, row_start, col_start, side, columns, first_column):
    row_hit = (
        lax.broadcasted_iota(jnp.int32, (1, MOS_ROWS, side), 1)
        == lax.broadcasted_iota(jnp.int32, (1, MOS_ROWS, side), 2) + row_start[:, None, None]
    ).astype(jnp.float32)
    col_hit = (
        lax.broadcasted_iota(jnp.int32, (1, side, columns), 2) + first_column
        == lax.broadcasted_iota(jnp.int32, (1, side, columns), 1) + col_start[:, None, None]
    ).astype(jnp.float32)
    rows_placed = jnp.einsum(
        "bri,cbij->bcrj", row_hit, values, precision=lax.Precision.HIGHEST,
        preferred_element_type=jnp.float32,
    )
    return jnp.einsum(
        "bcrj,bjk->crk", rows_placed, col_hit, precision=lax.Precision.HIGHEST,
        preferred_element_type=jnp.float32,
    )


def local(images, beam_weight, offsets, rejected_indicator, regression_indicator):
    ch_dev = images.shape[0]
    side = images.shape[2]
    col_dev = rejected_indicator.shape[2]
    all_channels = regression_indicator.shape[0]
    first_channel = lax.axis_index("chan") * ch_dev
    channel_ids = first_channel + jnp.arange(ch_dev, dtype=jnp.int32)
    exponent = 1.0 + 0.5 * channel_ids.astype(jnp.float32) / (all_channels - 1)
    row_start = jnp.clip(offsets[:, 0], 0, MOS_ROWS - side)
    col_start = jnp.clip(offsets[:, 1], 0, MOS_COLS - side)
    log_weight = jnp.log(beam_weight)

    core = lax.axis_index("chan") % 2
    half = side // 2
    own_half = lax.dynamic_slice_in_dim(log_weight, core * half, half, 1)
    corner = jnp.zeros((log_weight.shape[0], 8, side), jnp.float32)
    corner = corner.at[:, 0, 0].set(row_start.astype(jnp.float32))
    corner = corner.at[:, 0, 1].set(col_start.astype(jnp.float32))
    shared = lax.all_gather(jnp.concatenate([own_half, corner], axis=1), "beam", axis=0, tiled=True)
    chan_size = lax.psum(1, "chan")
    other = lax.ppermute(shared, "chan", [(a, a ^ 1) for a in range(chan_size)])
    first_half = jnp.where(core == 0, shared, other)
    second_half = jnp.where(core == 0, other, shared)
    every_log = jnp.concatenate([first_half[:, :half], second_half[:, :half]], axis=1)
    every_row = first_half[:, half, 0].astype(jnp.int32)
    every_col = first_half[:, half, 1].astype(jnp.int32)

    response = jnp.exp(exponent[:, None, None, None] * log_weight[None])
    numerator = place(response * images, row_start, col_start, side, MOS_COLS, 0)
    dividend_accumulator = lax.psum_scatter(numerator, "beam", scatter_dimension=2, tiled=True)

    every_response = jnp.exp(exponent[:, None, None, None] * every_log[None])
    col_first = lax.axis_index("beam") * col_dev
    normalizer_accumulated = place(
        every_response * every_response, every_row, every_col, side, col_dev, col_first
    )

    accepted_entries = 1.0 - rejected_indicator.astype(jnp.float32)
    emission_absent = lax.dynamic_slice_in_dim(regression_indicator, first_channel, ch_dev).astype(
        jnp.float32
    )
    celestial_image = accepted_entries * dividend_accumulator / normalizer_accumulated
    importance_factor = normalizer_accumulated * (
        emission_absent[:, None, None] * accepted_entries + 0.01
    )
    arrived = lax.all_to_all(
        jnp.stack([celestial_image, importance_factor]), "chan", split_axis=2, concat_axis=1, tiled=True
    )
    return clean_pair((arrived[0], arrived[1]))


def solution(mesh):
    in_specs = (
        P("chan", "beam", None, None),
        P("beam", None, None),
        P("beam", None),
        P("chan", None, "beam"),
        P(),
    )
    out_specs = P(None, "chan", "beam")
    return jax.shard_map(local, mesh=mesh, in_specs=in_specs, out_specs=out_specs, check_vma=False)
```

```python
import jax
import jax.numpy as jnp
from jax import lax
from jax.sharding import PartitionSpec as P

MOS_ROWS = 192
MOS_COLS = 512


def legendre(count):
    position = (2.0 * jnp.arange(count).astype(jnp.float32) + 1.0) / count - 1.0
    square = position * position
    return jnp.stack(
        [
            jnp.ones_like(position),
            position,
            0.5 * (3.0 * square - 1.0),
            0.5 * (5.0 * square * position - 3.0 * position),
        ],
        axis=1,
    )


def solve_cubic(normal_matrix, right_side):
    factor = {}
    for outer in range(4):
        for inner in range(outer + 1):
            value = normal_matrix[outer * 4 + inner]
            for other in range(inner):
                value = value - factor[outer, other] * factor[inner, other]
            if outer == inner:
                factor[outer, outer] = jnp.sqrt(value)
            else:
                factor[outer, inner] = value / factor[inner, inner]
    forward = []
    for outer in range(4):
        value = right_side[outer]
        for other in range(outer):
            value = value - factor[outer, other] * forward[other]
        forward.append(value / factor[outer, outer])
    backward = [None] * 4
    for outer in range(3, -1, -1):
        value = forward[outer]
        for other in range(outer + 1, 4):
            value = value - factor[other, outer] * backward[other]
        backward[outer] = value / factor[outer, outer]
    return jnp.stack(backward, axis=0)


def clean_pair(pair):
    sky_tile, weight_tile = pair
    channels, rows, columns = sky_tile.shape
    celestial_image = sky_tile.reshape(channels, rows * columns)
    importance_factor = weight_tile.reshape(channels, rows * columns)
    table = legendre(channels)
    products = jnp.stack(
        [table[:, outer] * table[:, inner] for outer in range(4) for inner in range(4)], axis=0
    )
    normal_matrix = jnp.dot(
        products,
        importance_factor,
        precision=lax.Precision.HIGHEST,
        preferred_element_type=jnp.float32,
    )
    right_side = jnp.dot(
        table.T,
        importance_factor * celestial_image,
        precision=lax.Precision.HIGHEST,
        preferred_element_type=jnp.float32,
    )
    coefficients = solve_cubic(normal_matrix, right_side)
    continuum = jnp.dot(
        table, coefficients, precision=lax.Precision.HIGHEST, preferred_element_type=jnp.float32
    )
    residual = celestial_image - continuum
    padded = jnp.pad(residual, ((1, 1), (0, 0)))
    smoothed = 0.25 * padded[:-2] + 0.5 * residual + 0.25 * padded[2:]
    return smoothed.reshape(channels, rows, columns)


def local(images, beam_weight, offsets, rejected_indicator, regression_indicator):
    ch_dev = images.shape[0]
    side = images.shape[2]
    all_channels = regression_indicator.shape[0]
    first_channel = lax.axis_index("chan") * ch_dev
    channel_ids = first_channel + jnp.arange(ch_dev, dtype=jnp.int32)
    exponent = 1.0 + 0.5 * channel_ids.astype(jnp.float32) / (all_channels - 1)
    log_weight = jnp.log(beam_weight)
    response = jnp.exp(exponent[:, None, None, None] * log_weight[None])
    stacked = jnp.stack([response * images, response * response])
    row_start = jnp.clip(offsets[:, 0], 0, MOS_ROWS - side)
    col_start = jnp.clip(offsets[:, 1], 0, MOS_COLS - side)
    row_hit = (
        lax.broadcasted_iota(jnp.int32, (1, MOS_ROWS, side), 1)
        == lax.broadcasted_iota(jnp.int32, (1, MOS_ROWS, side), 2) + row_start[:, None, None]
    ).astype(jnp.float32)
    col_hit = (
        lax.broadcasted_iota(jnp.int32, (1, side, MOS_COLS), 2)
        == lax.broadcasted_iota(jnp.int32, (1, side, MOS_COLS), 1) + col_start[:, None, None]
    ).astype(jnp.float32)
    rows_placed = jnp.einsum(
        "bri,acbij->bacrj", row_hit, stacked, precision=lax.Precision.HIGHEST,
        preferred_element_type=jnp.float32,
    )
    blocks = lax.psum(1, "beam")
    col_hit = col_hit.reshape(col_hit.shape[0], side, blocks, MOS_COLS // blocks)
    planes = jnp.einsum(
        "bacrj,bjnk->nacrk", rows_placed, col_hit, precision=lax.Precision.HIGHEST,
        preferred_element_type=jnp.float32,
    )
    own = lax.psum_scatter(planes, "beam", scatter_dimension=0, tiled=False)
    dividend_accumulator = own[0]
    normalizer_accumulated = own[1]
    accepted_entries = 1.0 - rejected_indicator.astype(jnp.float32)
    emission_absent = lax.dynamic_slice_in_dim(regression_indicator, first_channel, ch_dev).astype(
        jnp.float32
    )
    celestial_image = accepted_entries * dividend_accumulator / normalizer_accumulated
    importance_factor = normalizer_accumulated * (
        emission_absent[:, None, None] * accepted_entries + 0.01
    )
    arrived = lax.all_to_all(
        jnp.stack([celestial_image, importance_factor]), "chan", split_axis=2, concat_axis=1, tiled=True
    )
    return clean_pair((arrived[0], arrived[1]))


def solution(mesh):
    in_specs = (
        P("chan", "beam", None, None),
        P("beam", None, None),
        P("beam", None),
        P("chan", None, "beam"),
        P(),
    )
    out_specs = P(None, "chan", "beam")
    return jax.shard_map(local, mesh=mesh, in_specs=in_specs, out_specs=out_specs, check_vma=False)
```

```python
import jax
import jax.numpy as jnp
from jax import lax
from jax.sharding import PartitionSpec as P

MOS_ROWS = 192
MOS_COLS = 512


def legendre(count):
    position = (2.0 * jnp.arange(count).astype(jnp.float32) + 1.0) / count - 1.0
    square = position * position
    return jnp.stack(
        [
            jnp.ones_like(position),
            position,
            0.5 * (3.0 * square - 1.0),
            0.5 * (5.0 * square * position - 3.0 * position),
        ],
        axis=1,
    )


def solve_cubic(normal_matrix, right_side):
    factor = {}
    for outer in range(4):
        for inner in range(outer + 1):
            value = normal_matrix[outer * 4 + inner]
            for other in range(inner):
                value = value - factor[outer, other] * factor[inner, other]
            if outer == inner:
                factor[outer, outer] = jnp.sqrt(value)
            else:
                factor[outer, inner] = value / factor[inner, inner]
    forward = []
    for outer in range(4):
        value = right_side[outer]
        for other in range(outer):
            value = value - factor[outer, other] * forward[other]
        forward.append(value / factor[outer, outer])
    backward = [None] * 4
    for outer in range(3, -1, -1):
        value = forward[outer]
        for other in range(outer + 1, 4):
            value = value - factor[other, outer] * backward[other]
        backward[outer] = value / factor[outer, outer]
    return jnp.stack(backward, axis=0)


def clean_pair(pair):
    sky_tile, weight_tile = pair
    channels, rows, columns = sky_tile.shape
    celestial_image = sky_tile.reshape(channels, rows * columns)
    importance_factor = weight_tile.reshape(channels, rows * columns)
    table = legendre(channels)
    products = jnp.stack(
        [table[:, outer] * table[:, inner] for outer in range(4) for inner in range(4)], axis=0
    )
    normal_matrix = jnp.dot(
        products,
        importance_factor,
        precision=lax.Precision.HIGHEST,
        preferred_element_type=jnp.float32,
    )
    right_side = jnp.dot(
        table.T,
        importance_factor * celestial_image,
        precision=lax.Precision.HIGHEST,
        preferred_element_type=jnp.float32,
    )
    coefficients = solve_cubic(normal_matrix, right_side)
    continuum = jnp.dot(
        table, coefficients, precision=lax.Precision.HIGHEST, preferred_element_type=jnp.float32
    )
    residual = celestial_image - continuum
    padded = jnp.pad(residual, ((1, 1), (0, 0)))
    smoothed = 0.25 * padded[:-2] + 0.5 * residual + 0.25 * padded[2:]
    return smoothed.reshape(channels, rows, columns)


def line_all_gather(piece):
    groups = lax.psum(1, "beam")
    me = lax.axis_index("beam")
    from_left = [piece]
    from_right = [piece]
    for step in range(1, groups):
        from_left.append(
            lax.ppermute(from_left[-1], "beam", [(i, i + 1) for i in range(step - 1, groups - 1)])
        )
        from_right.append(
            lax.ppermute(from_right[-1], "beam", [(i, i - 1) for i in range(1, groups - step + 1)])
        )
    gathered = []
    for group in range(groups):
        chosen = piece
        for step in range(1, groups):
            chosen = jnp.where(me - step == group, from_left[step], chosen)
            chosen = jnp.where(me + step == group, from_right[step], chosen)
        gathered.append(chosen)
    return jnp.concatenate(gathered, axis=0)


def place(values, row_start, col_start, side, columns, first_column):
    row_hit = (
        lax.broadcasted_iota(jnp.int32, (1, MOS_ROWS, side), 1)
        == lax.broadcasted_iota(jnp.int32, (1, MOS_ROWS, side), 2) + row_start[:, None, None]
    ).astype(jnp.float32)
    col_hit = (
        lax.broadcasted_iota(jnp.int32, (1, side, columns), 2) + first_column
        == lax.broadcasted_iota(jnp.int32, (1, side, columns), 1) + col_start[:, None, None]
    ).astype(jnp.float32)
    rows_placed = jnp.einsum(
        "bri,cbij->bcrj", row_hit, values, precision=lax.Precision.HIGHEST,
        preferred_element_type=jnp.float32,
    )
    return jnp.einsum(
        "bcrj,bjk->crk", rows_placed, col_hit, precision=lax.Precision.HIGHEST,
        preferred_element_type=jnp.float32,
    )


def local(images, beam_weight, offsets, rejected_indicator, regression_indicator):
    ch_dev = images.shape[0]
    side = images.shape[2]
    col_dev = rejected_indicator.shape[2]
    all_channels = regression_indicator.shape[0]
    first_channel = lax.axis_index("chan") * ch_dev
    channel_ids = first_channel + jnp.arange(ch_dev, dtype=jnp.int32)
    exponent = 1.0 + 0.5 * channel_ids.astype(jnp.float32) / (all_channels - 1)
    row_start = jnp.clip(offsets[:, 0], 0, MOS_ROWS - side)
    col_start = jnp.clip(offsets[:, 1], 0, MOS_COLS - side)
    log_weight = jnp.log(beam_weight)

    core = lax.axis_index("chan") % 2
    half = side // 2
    own_half = lax.dynamic_slice_in_dim(log_weight, core * half, half, 1)
    corner = jnp.zeros((log_weight.shape[0], 8, side), jnp.float32)
    corner = corner.at[:, 0, 0].set(row_start.astype(jnp.float32))
    corner = corner.at[:, 0, 1].set(col_start.astype(jnp.float32))
    shared = line_all_gather(jnp.concatenate([own_half, corner], axis=1))
    chan_size = lax.psum(1, "chan")
    other = lax.ppermute(shared, "chan", [(a, a ^ 1) for a in range(chan_size)])
    first_half = jnp.where(core == 0, shared, other)
    second_half = jnp.where(core == 0, other, shared)
    every_log = jnp.concatenate([first_half[:, :half], second_half[:, :half]], axis=1)
    every_row = first_half[:, half, 0].astype(jnp.int32)
    every_col = first_half[:, half, 1].astype(jnp.int32)

    response = jnp.exp(exponent[:, None, None, None] * log_weight[None])
    numerator = place(response * images, row_start, col_start, side, MOS_COLS, 0)
    dividend_accumulator = lax.psum_scatter(numerator, "beam", scatter_dimension=2, tiled=True)

    every_response = jnp.exp(exponent[:, None, None, None] * every_log[None])
    col_first = lax.axis_index("beam") * col_dev
    normalizer_accumulated = place(
        every_response * every_response, every_row, every_col, side, col_dev, col_first
    )

    accepted_entries = 1.0 - rejected_indicator.astype(jnp.float32)
    emission_absent = lax.dynamic_slice_in_dim(regression_indicator, first_channel, ch_dev).astype(
        jnp.float32
    )
    celestial_image = accepted_entries * dividend_accumulator / normalizer_accumulated
    importance_factor = normalizer_accumulated * (
        emission_absent[:, None, None] * accepted_entries + 0.01
    )
    arrived = lax.all_to_all(
        jnp.stack([celestial_image, importance_factor]), "chan", split_axis=2, concat_axis=1, tiled=True
    )
    return clean_pair((arrived[0], arrived[1]))


def solution(mesh):
    in_specs = (
        P("chan", "beam", None, None),
        P("beam", None, None),
        P("beam", None),
        P("chan", None, "beam"),
        P(),
    )
    out_specs = P(None, "chan", "beam")
    return jax.shard_map(local, mesh=mesh, in_specs=in_specs, out_specs=out_specs, check_vma=False)
```

```python
import jax
import numpy as np
import jax.numpy as jnp
from jax import lax
from jax.sharding import PartitionSpec as P


MOS_ROWS = 192
MOS_COLS = 512


def legendre(count):
    position = (2.0 * jnp.arange(count).astype(jnp.float32) + 1.0) / count - 1.0
    square = position * position
    return jnp.stack(
        [
            jnp.ones_like(position),
            position,
            0.5 * (3.0 * square - 1.0),
            0.5 * (5.0 * square * position - 3.0 * position),
        ],
        axis=1,
    )


def solve_cubic(normal_matrix, right_side):
    factor = {}
    for outer in range(4):
        for inner in range(outer + 1):
            value = normal_matrix[outer * 4 + inner]
            for other in range(inner):
                value = value - factor[outer, other] * factor[inner, other]
            if outer == inner:
                factor[outer, outer] = jnp.sqrt(value)
            else:
                factor[outer, inner] = value / factor[inner, inner]
    forward = []
    for outer in range(4):
        value = right_side[outer]
        for other in range(outer):
            value = value - factor[outer, other] * forward[other]
        forward.append(value / factor[outer, outer])
    backward = [None] * 4
    for outer in range(3, -1, -1):
        value = forward[outer]
        for other in range(outer + 1, 4):
            value = value - factor[other, outer] * backward[other]
        backward[outer] = value / factor[outer, outer]
    return jnp.stack(backward, axis=0)


def clean_pair(pair):
    sky_tile, weight_tile = pair
    channels, rows, columns = sky_tile.shape
    celestial_image = sky_tile.reshape(channels, rows * columns)
    importance_factor = weight_tile.reshape(channels, rows * columns)
    table = legendre(channels)
    products = jnp.stack(
        [table[:, outer] * table[:, inner] for outer in range(4) for inner in range(4)], axis=0
    )
    normal_matrix = jnp.dot(
        products,
        importance_factor,
        precision=lax.Precision.HIGHEST,
        preferred_element_type=jnp.float32,
    )
    right_side = jnp.dot(
        table.T,
        importance_factor * celestial_image,
        precision=lax.Precision.HIGHEST,
        preferred_element_type=jnp.float32,
    )
    coefficients = solve_cubic(normal_matrix, right_side)
    continuum = jnp.dot(
        table, coefficients, precision=lax.Precision.HIGHEST, preferred_element_type=jnp.float32
    )
    residual = celestial_image - continuum
    padded = jnp.pad(residual, ((1, 1), (0, 0)))
    smoothed = 0.25 * padded[:-2] + 0.5 * residual + 0.25 * padded[2:]
    return smoothed.reshape(channels, rows, columns)


JITTER = 16


def reaching_beams(groups, beams, side):
    grid = int(round(beams ** 0.5))
    block = MOS_COLS // groups
    lists = []
    for target in range(groups):
        found = []
        for beam in range(beams):
            col = beam % grid
            base = col * (MOS_COLS - side) // (grid - 1)
            inner = 0 < col < grid - 1
            low = max(base - JITTER, 0) if inner else base
            high = min(base + JITTER, MOS_COLS - side) if inner else base
            if low < block * (target + 1) and high + side > block * target:
                found.append(beam)
        lists.append(found)
    width = max(len(found) for found in lists)
    table = np.array([found + [0] * (width - len(found)) for found in lists], np.int32)
    valid = np.array([[True] * len(found) + [False] * (width - len(found)) for found in lists])
    return table, valid


def line_all_gather(piece):
    groups = lax.psum(1, "beam")
    me = lax.axis_index("beam")
    from_left = [piece]
    from_right = [piece]
    for step in range(1, groups):
        from_left.append(
            lax.ppermute(from_left[-1], "beam", [(i, i + 1) for i in range(step - 1, groups - 1)])
        )
        from_right.append(
            lax.ppermute(from_right[-1], "beam", [(i, i - 1) for i in range(1, groups - step + 1)])
        )
    gathered = []
    for group in range(groups):
        chosen = piece
        for step in range(1, groups):
            chosen = jnp.where(me - step == group, from_left[step], chosen)
            chosen = jnp.where(me + step == group, from_right[step], chosen)
        gathered.append(chosen)
    return jnp.concatenate(gathered, axis=0)


def place(values, row_start, col_start, side, columns, first_column):
    row_hit = (
        lax.broadcasted_iota(jnp.int32, (1, MOS_ROWS, side), 1)
        == lax.broadcasted_iota(jnp.int32, (1, MOS_ROWS, side), 2) + row_start[:, None, None]
    ).astype(jnp.float32)
    col_hit = (
        lax.broadcasted_iota(jnp.int32, (1, side, columns), 2) + first_column
        == lax.broadcasted_iota(jnp.int32, (1, side, columns), 1) + col_start[:, None, None]
    ).astype(jnp.float32)
    rows_placed = jnp.einsum(
        "bri,cbij->bcrj", row_hit, values, precision=lax.Precision.HIGHEST,
        preferred_element_type=jnp.float32,
    )
    return jnp.einsum(
        "bcrj,bjk->crk", rows_placed, col_hit, precision=lax.Precision.HIGHEST,
        preferred_element_type=jnp.float32,
    )


def local_body(images, beam_weight, offsets, rejected_indicator, regression_indicator):
    ch_dev = images.shape[0]
    side = images.shape[2]
    col_dev = rejected_indicator.shape[2]
    all_channels = regression_indicator.shape[0]
    first_channel = lax.axis_index("chan") * ch_dev
    channel_ids = first_channel + jnp.arange(ch_dev, dtype=jnp.int32)
    exponent = 1.0 + 0.5 * channel_ids.astype(jnp.float32) / (all_channels - 1)
    row_start = jnp.clip(offsets[:, 0], 0, MOS_ROWS - side)
    col_start = jnp.clip(offsets[:, 1], 0, MOS_COLS - side)
    log_weight = jnp.log(beam_weight)

    core = lax.axis_index("chan") % 2
    half = side // 2
    own_half = lax.dynamic_slice_in_dim(log_weight, core * half, half, 1)
    corner = jnp.zeros((log_weight.shape[0], 8, side), jnp.float32)
    corner = corner.at[:, 0, 0].set(row_start.astype(jnp.float32))
    corner = corner.at[:, 0, 1].set(col_start.astype(jnp.float32))
    response = jnp.exp(exponent[:, None, None, None] * log_weight[None])
    numerator = place(response * images, row_start, col_start, side, MOS_COLS, 0)
    numerator, outgoing = lax.optimization_barrier(
        (numerator, jnp.concatenate([own_half, corner], axis=1))
    )
    dividend_accumulator = lax.psum_scatter(numerator, "beam", scatter_dimension=2, tiled=True)
    shared = line_all_gather(outgoing)
    chan_size = lax.psum(1, "chan")
    other = lax.ppermute(shared, "chan", [(a, a ^ 1) for a in range(chan_size)])
    first_half = jnp.where(core == 0, shared, other)
    second_half = jnp.where(core == 0, other, shared)
    every_log = jnp.concatenate([first_half[:, :half], second_half[:, :half]], axis=1)
    every_row = first_half[:, half, 0].astype(jnp.int32)
    every_col = first_half[:, half, 1].astype(jnp.int32)
    table, valid = reaching_beams(lax.psum(1, "beam"), every_log.shape[0], side)
    me = lax.axis_index("beam")
    chosen = jnp.asarray(table)[me]
    every_log = jnp.take(every_log, chosen, axis=0)
    every_row = jnp.take(every_row, chosen, axis=0)
    every_col = jnp.where(jnp.asarray(valid)[me], jnp.take(every_col, chosen, axis=0), -4 * MOS_COLS)

    every_response = jnp.exp(exponent[:, None, None, None] * every_log[None])
    col_first = lax.axis_index("beam") * col_dev
    normalizer_accumulated = place(
        every_response * every_response, every_row, every_col, side, col_dev, col_first
    )

    normalizer_accumulated = lax.optimization_barrier(normalizer_accumulated)
    accepted_entries = 1.0 - rejected_indicator.astype(jnp.float32)
    emission_absent = lax.dynamic_slice_in_dim(regression_indicator, first_channel, ch_dev).astype(
        jnp.float32
    )
    celestial_image = accepted_entries * dividend_accumulator / normalizer_accumulated
    importance_factor = normalizer_accumulated * (
        emission_absent[:, None, None] * accepted_entries + 0.01
    )
    arrived = lax.all_to_all(
        jnp.stack([celestial_image, importance_factor]), "chan", split_axis=2, concat_axis=1, tiled=True
    )
    return clean_pair((arrived[0], arrived[1]))


def solution(mesh):
    in_specs = (
        P("chan", "beam", None, None),
        P("beam", None, None),
        P("beam", None),
        P("chan", None, "beam"),
        P(),
    )
    out_specs = P(None, "chan", "beam")
    return jax.shard_map(local_body, mesh=mesh, in_specs=in_specs, out_specs=out_specs, check_vma=False)
```

```python
import jax
import jax.numpy as jnp
from jax import lax
from jax.sharding import PartitionSpec as P

MOS_ROWS = 192
MOS_COLS = 512


def legendre(count):
    position = (2.0 * jnp.arange(count).astype(jnp.float32) + 1.0) / count - 1.0
    square = position * position
    return jnp.stack(
        [
            jnp.ones_like(position),
            position,
            0.5 * (3.0 * square - 1.0),
            0.5 * (5.0 * square * position - 3.0 * position),
        ],
        axis=1,
    )


def solve_cubic(normal_matrix, right_side):
    factor = {}
    for outer in range(4):
        for inner in range(outer + 1):
            value = normal_matrix[outer * 4 + inner]
            for other in range(inner):
                value = value - factor[outer, other] * factor[inner, other]
            if outer == inner:
                factor[outer, outer] = jnp.sqrt(value)
            else:
                factor[outer, inner] = value / factor[inner, inner]
    forward = []
    for outer in range(4):
        value = right_side[outer]
        for other in range(outer):
            value = value - factor[outer, other] * forward[other]
        forward.append(value / factor[outer, outer])
    backward = [None] * 4
    for outer in range(3, -1, -1):
        value = forward[outer]
        for other in range(outer + 1, 4):
            value = value - factor[other, outer] * backward[other]
        backward[outer] = value / factor[outer, outer]
    return jnp.stack(backward, axis=0)


def clean_pair(pair):
    sky_tile, weight_tile = pair
    channels, rows, columns = sky_tile.shape
    celestial_image = sky_tile.reshape(channels, rows * columns)
    importance_factor = weight_tile.reshape(channels, rows * columns)
    table = legendre(channels)
    products = jnp.stack(
        [table[:, outer] * table[:, inner] for outer in range(4) for inner in range(4)], axis=0
    )
    normal_matrix = jnp.dot(
        products,
        importance_factor,
        precision=lax.Precision.HIGHEST,
        preferred_element_type=jnp.float32,
    )
    right_side = jnp.dot(
        table.T,
        importance_factor * celestial_image,
        precision=lax.Precision.HIGHEST,
        preferred_element_type=jnp.float32,
    )
    coefficients = solve_cubic(normal_matrix, right_side)
    continuum = jnp.dot(
        table, coefficients, precision=lax.Precision.HIGHEST, preferred_element_type=jnp.float32
    )
    residual = celestial_image - continuum
    padded = jnp.pad(residual, ((1, 1), (0, 0)))
    smoothed = 0.25 * padded[:-2] + 0.5 * residual + 0.25 * padded[2:]
    return smoothed.reshape(channels, rows, columns)


def local(images, beam_weight, offsets, rejected_indicator, regression_indicator):
    ch_dev = images.shape[0]
    side = images.shape[2]
    all_channels = regression_indicator.shape[0]
    first_channel = lax.axis_index("chan") * ch_dev
    channel_ids = first_channel + jnp.arange(ch_dev, dtype=jnp.int32)
    exponent = 1.0 + 0.5 * channel_ids.astype(jnp.float32) / (all_channels - 1)
    log_weight = jnp.log(beam_weight)
    response = jnp.exp(exponent[:, None, None, None] * log_weight[None])
    stacked = jnp.stack([response * images, response * response])
    row_start = jnp.clip(offsets[:, 0], 0, MOS_ROWS - side)
    col_start = jnp.clip(offsets[:, 1], 0, MOS_COLS - side)
    row_hit = (
        lax.broadcasted_iota(jnp.int32, (1, MOS_ROWS, side), 1)
        == lax.broadcasted_iota(jnp.int32, (1, MOS_ROWS, side), 2) + row_start[:, None, None]
    ).astype(jnp.float32)
    col_hit = (
        lax.broadcasted_iota(jnp.int32, (1, side, MOS_COLS), 2)
        == lax.broadcasted_iota(jnp.int32, (1, side, MOS_COLS), 1) + col_start[:, None, None]
    ).astype(jnp.float32)
    rows_placed = jnp.einsum(
        "bri,acbij->bacrj", row_hit, stacked, precision=lax.Precision.HIGH,
        preferred_element_type=jnp.float32,
    )
    blocks = lax.psum(1, "beam")
    col_hit = col_hit.reshape(col_hit.shape[0], side, blocks, MOS_COLS // blocks)
    planes = jnp.einsum(
        "bacrj,bjnk->nacrk", rows_placed, col_hit, precision=lax.Precision.HIGH,
        preferred_element_type=jnp.float32,
    )
    own = lax.psum_scatter(planes, "beam", scatter_dimension=0, tiled=False)
    dividend_accumulator = own[0]
    normalizer_accumulated = own[1]
    accepted_entries = 1.0 - rejected_indicator.astype(jnp.float32)
    emission_absent = lax.dynamic_slice_in_dim(regression_indicator, first_channel, ch_dev).astype(
        jnp.float32
    )
    celestial_image = accepted_entries * dividend_accumulator / normalizer_accumulated
    importance_factor = normalizer_accumulated * (
        emission_absent[:, None, None] * accepted_entries + 0.01
    )
    arrived = lax.all_to_all(
        jnp.stack([celestial_image, importance_factor]), "chan", split_axis=2, concat_axis=1, tiled=True
    )
    return clean_pair((arrived[0], arrived[1]))


def solution(mesh):
    in_specs = (
        P("chan", "beam", None, None),
        P("beam", None, None),
        P("beam", None),
        P("chan", None, "beam"),
        P(),
    )
    out_specs = P(None, "chan", "beam")
    return jax.shard_map(local, mesh=mesh, in_specs=in_specs, out_specs=out_specs, check_vma=False)
```

```python
import jax
import jax.numpy as jnp
from jax import lax
from jax.sharding import PartitionSpec as P

MOS_ROWS = 192
MOS_COLS = 512


def legendre(count):
    position = (2.0 * jnp.arange(count).astype(jnp.float32) + 1.0) / count - 1.0
    square = position * position
    return jnp.stack(
        [
            jnp.ones_like(position),
            position,
            0.5 * (3.0 * square - 1.0),
            0.5 * (5.0 * square * position - 3.0 * position),
        ],
        axis=1,
    )


def solve_cubic(normal_matrix, right_side):
    factor = {}
    for outer in range(4):
        for inner in range(outer + 1):
            value = normal_matrix[outer * 4 + inner]
            for other in range(inner):
                value = value - factor[outer, other] * factor[inner, other]
            if outer == inner:
                factor[outer, outer] = jnp.sqrt(value)
            else:
                factor[outer, inner] = value / factor[inner, inner]
    forward = []
    for outer in range(4):
        value = right_side[outer]
        for other in range(outer):
            value = value - factor[outer, other] * forward[other]
        forward.append(value / factor[outer, outer])
    backward = [None] * 4
    for outer in range(3, -1, -1):
        value = forward[outer]
        for other in range(outer + 1, 4):
            value = value - factor[other, outer] * backward[other]
        backward[outer] = value / factor[outer, outer]
    return jnp.stack(backward, axis=0)


def clean_pair(pair):
    sky_tile, weight_tile = pair
    channels, rows, columns = sky_tile.shape
    celestial_image = sky_tile.reshape(channels, rows * columns)
    importance_factor = weight_tile.reshape(channels, rows * columns)
    table = legendre(channels)
    products = jnp.stack(
        [table[:, outer] * table[:, inner] for outer in range(4) for inner in range(4)], axis=0
    )
    normal_matrix = jnp.dot(
        products,
        importance_factor,
        precision=lax.Precision.HIGHEST,
        preferred_element_type=jnp.float32,
    )
    right_side = jnp.dot(
        table.T,
        importance_factor * celestial_image,
        precision=lax.Precision.HIGHEST,
        preferred_element_type=jnp.float32,
    )
    coefficients = solve_cubic(normal_matrix, right_side)
    continuum = jnp.dot(
        table, coefficients, precision=lax.Precision.HIGHEST, preferred_element_type=jnp.float32
    )
    residual = celestial_image - continuum
    padded = jnp.pad(residual, ((1, 1), (0, 0)))
    smoothed = 0.25 * padded[:-2] + 0.5 * residual + 0.25 * padded[2:]
    return smoothed.reshape(channels, rows, columns)


def exact_onehot_dot(spec, first, second, data_first):
    data = first if data_first else second
    wide = lax.reduce_precision(data, exponent_bits=8, mantissa_bits=15)
    rest = data - wide
    parts = []
    for piece, precision in ((wide, lax.Precision.HIGH), (rest, lax.Precision.DEFAULT)):
        operands = (piece, second) if data_first else (first, piece)
        parts.append(
            jnp.einsum(spec, *operands, precision=precision, preferred_element_type=jnp.float32)
        )
    return parts[0] + parts[1]


def local(images, beam_weight, offsets, rejected_indicator, regression_indicator):
    ch_dev = images.shape[0]
    side = images.shape[2]
    all_channels = regression_indicator.shape[0]
    first_channel = lax.axis_index("chan") * ch_dev
    channel_ids = first_channel + jnp.arange(ch_dev, dtype=jnp.int32)
    exponent = 1.0 + 0.5 * channel_ids.astype(jnp.float32) / (all_channels - 1)
    log_weight = jnp.log(beam_weight)
    response = jnp.exp(exponent[:, None, None, None] * log_weight[None])
    stacked = jnp.stack([response * images, response * response])
    row_start = jnp.clip(offsets[:, 0], 0, MOS_ROWS - side)
    col_start = jnp.clip(offsets[:, 1], 0, MOS_COLS - side)
    row_hit = (
        lax.broadcasted_iota(jnp.int32, (1, MOS_ROWS, side), 1)
        == lax.broadcasted_iota(jnp.int32, (1, MOS_ROWS, side), 2) + row_start[:, None, None]
    ).astype(jnp.float32)
    col_hit = (
        lax.broadcasted_iota(jnp.int32, (1, side, MOS_COLS), 2)
        == lax.broadcasted_iota(jnp.int32, (1, side, MOS_COLS), 1) + col_start[:, None, None]
    ).astype(jnp.float32)
    rows_placed = exact_onehot_dot("bri,acbij->bacrj", row_hit, stacked, data_first=False)
    blocks = lax.psum(1, "beam")
    col_hit = col_hit.reshape(col_hit.shape[0], side, blocks, MOS_COLS // blocks)
    planes = exact_onehot_dot("bacrj,bjnk->nacrk", rows_placed, col_hit, data_first=True)
    own = lax.psum_scatter(planes, "beam", scatter_dimension=0, tiled=False)
    dividend_accumulator = own[0]
    normalizer_accumulated = own[1]
    accepted_entries = 1.0 - rejected_indicator.astype(jnp.float32)
    emission_absent = lax.dynamic_slice_in_dim(regression_indicator, first_channel, ch_dev).astype(
        jnp.float32
    )
    celestial_image = accepted_entries * dividend_accumulator / normalizer_accumulated
    importance_factor = normalizer_accumulated * (
        emission_absent[:, None, None] * accepted_entries + 0.01
    )
    arrived = lax.all_to_all(
        jnp.stack([celestial_image, importance_factor]), "chan", split_axis=2, concat_axis=1, tiled=True
    )
    return clean_pair((arrived[0], arrived[1]))


def solution(mesh):
    in_specs = (
        P("chan", "beam", None, None),
        P("beam", None, None),
        P("beam", None),
        P("chan", None, "beam"),
        P(),
    )
    out_specs = P(None, "chan", "beam")
    return jax.shard_map(local, mesh=mesh, in_specs=in_specs, out_specs=out_specs, check_vma=False)
```

```python
import jax
import jax.numpy as jnp
from jax import lax
from jax.sharding import PartitionSpec as P

MOS_ROWS = 192
MOS_COLS = 512


def legendre(count):
    position = (2.0 * jnp.arange(count).astype(jnp.float32) + 1.0) / count - 1.0
    square = position * position
    return jnp.stack(
        [
            jnp.ones_like(position),
            position,
            0.5 * (3.0 * square - 1.0),
            0.5 * (5.0 * square * position - 3.0 * position),
        ],
        axis=1,
    )


def solve_cubic(normal_matrix, right_side):
    factor = {}
    for outer in range(4):
        for inner in range(outer + 1):
            value = normal_matrix[outer * 4 + inner]
            for other in range(inner):
                value = value - factor[outer, other] * factor[inner, other]
            if outer == inner:
                factor[outer, outer] = jnp.sqrt(value)
            else:
                factor[outer, inner] = value / factor[inner, inner]
    forward = []
    for outer in range(4):
        value = right_side[outer]
        for other in range(outer):
            value = value - factor[outer, other] * forward[other]
        forward.append(value / factor[outer, outer])
    backward = [None] * 4
    for outer in range(3, -1, -1):
        value = forward[outer]
        for other in range(outer + 1, 4):
            value = value - factor[other, outer] * backward[other]
        backward[outer] = value / factor[outer, outer]
    return jnp.stack(backward, axis=0)


def clean_pair(pair):
    sky_tile, weight_tile = pair
    channels, rows, columns = sky_tile.shape
    celestial_image = sky_tile.reshape(channels, rows * columns)
    importance_factor = weight_tile.reshape(channels, rows * columns)
    table = legendre(channels)
    products = jnp.stack(
        [table[:, outer] * table[:, inner] for outer in range(4) for inner in range(4)], axis=0
    )
    normal_matrix = jnp.dot(
        products,
        importance_factor,
        precision=lax.Precision.HIGHEST,
        preferred_element_type=jnp.float32,
    )
    right_side = jnp.dot(
        table.T,
        importance_factor * celestial_image,
        precision=lax.Precision.HIGHEST,
        preferred_element_type=jnp.float32,
    )
    coefficients = solve_cubic(normal_matrix, right_side)
    continuum = jnp.dot(
        table, coefficients, precision=lax.Precision.HIGHEST, preferred_element_type=jnp.float32
    )
    residual = celestial_image - continuum
    padded = jnp.pad(residual, ((1, 1), (0, 0)))
    smoothed = 0.25 * padded[:-2] + 0.5 * residual + 0.25 * padded[2:]
    return smoothed.reshape(channels, rows, columns)


def local(images, beam_weight, offsets, rejected_indicator, regression_indicator):
    ch_dev = images.shape[0]
    side = images.shape[2]
    all_channels = regression_indicator.shape[0]
    first_channel = lax.axis_index("chan") * ch_dev
    channel_ids = first_channel + jnp.arange(ch_dev, dtype=jnp.int32)
    exponent = 1.0 + 0.5 * channel_ids.astype(jnp.float32) / (all_channels - 1)
    log_weight = jnp.log(beam_weight)
    response = jnp.exp(exponent[:, None, None, None] * log_weight[None])
    stacked = jnp.stack([response * images, response * response])
    row_start = jnp.clip(offsets[:, 0], 0, MOS_ROWS - side)
    col_start = jnp.clip(offsets[:, 1], 0, MOS_COLS - side)
    row_hit = (
        lax.broadcasted_iota(jnp.int32, (1, MOS_ROWS, side), 1)
        == lax.broadcasted_iota(jnp.int32, (1, MOS_ROWS, side), 2) + row_start[:, None, None]
    ).astype(jnp.float32)
    col_hit = (
        lax.broadcasted_iota(jnp.int32, (1, side, MOS_COLS), 2)
        == lax.broadcasted_iota(jnp.int32, (1, side, MOS_COLS), 1) + col_start[:, None, None]
    ).astype(jnp.float32)
    rows_placed = jnp.einsum(
        "bri,acbij->bacrj", row_hit, stacked, precision=lax.Precision.HIGHEST,
        preferred_element_type=jnp.float32,
    )
    blocks = lax.psum(1, "beam")
    col_hit = col_hit.reshape(col_hit.shape[0], side, blocks, MOS_COLS // blocks)
    planes = jnp.einsum(
        "bacrj,bjnk->nacrk", rows_placed, col_hit, precision=lax.Precision.HIGHEST,
        preferred_element_type=jnp.float32,
    )
    own = lax.psum_scatter(planes, "beam", scatter_dimension=0, tiled=False)
    dividend_accumulator = own[0]
    normalizer_accumulated = own[1]
    accepted_entries = 1.0 - rejected_indicator.astype(jnp.float32)
    emission_absent = lax.dynamic_slice_in_dim(regression_indicator, first_channel, ch_dev).astype(
        jnp.float32
    )
    celestial_image = accepted_entries * dividend_accumulator / normalizer_accumulated
    importance_factor = normalizer_accumulated * (
        emission_absent[:, None, None] * accepted_entries + 0.01
    )
    both = jnp.stack([celestial_image, importance_factor])
    kinds, chans, rows, cols = both.shape
    both = both.transpose(2, 0, 1, 3).reshape(rows, kinds * chans, cols)
    both = lax.all_to_all(both, "chan", split_axis=0, concat_axis=0, tiled=True)
    sources = all_channels // chans
    rows_dev = rows // sources
    both = both.reshape(sources, rows_dev, kinds, chans, cols).transpose(2, 0, 3, 1, 4)
    both = both.reshape(kinds, all_channels, rows_dev, cols)
    return clean_pair((both[0], both[1]))


def solution(mesh):
    in_specs = (
        P("chan", "beam", None, None),
        P("beam", None, None),
        P("beam", None),
        P("chan", None, "beam"),
        P(),
    )
    out_specs = P(None, "chan", "beam")
    return jax.shard_map(local, mesh=mesh, in_specs=in_specs, out_specs=out_specs, check_vma=False)
```

```python
import jax
import jax.numpy as jnp
from jax import lax
from jax.sharding import PartitionSpec as P

MOS_ROWS = 192
MOS_COLS = 512


def legendre(count):
    position = (2.0 * jnp.arange(count).astype(jnp.float32) + 1.0) / count - 1.0
    square = position * position
    return jnp.stack(
        [
            jnp.ones_like(position),
            position,
            0.5 * (3.0 * square - 1.0),
            0.5 * (5.0 * square * position - 3.0 * position),
        ],
        axis=1,
    )


def solve_cubic(normal_matrix, right_side):
    factor = {}
    for outer in range(4):
        for inner in range(outer + 1):
            value = normal_matrix[outer * 4 + inner]
            for other in range(inner):
                value = value - factor[outer, other] * factor[inner, other]
            if outer == inner:
                factor[outer, outer] = jnp.sqrt(value)
            else:
                factor[outer, inner] = value / factor[inner, inner]
    forward = []
    for outer in range(4):
        value = right_side[outer]
        for other in range(outer):
            value = value - factor[outer, other] * forward[other]
        forward.append(value / factor[outer, outer])
    backward = [None] * 4
    for outer in range(3, -1, -1):
        value = forward[outer]
        for other in range(outer + 1, 4):
            value = value - factor[other, outer] * backward[other]
        backward[outer] = value / factor[outer, outer]
    return jnp.stack(backward, axis=0)


def clean_pair(pair):
    sky_tile, weight_tile = pair
    channels, rows, columns = sky_tile.shape
    celestial_image = sky_tile.reshape(channels, rows * columns)
    importance_factor = weight_tile.reshape(channels, rows * columns)
    table = legendre(channels)
    products = jnp.stack(
        [table[:, outer] * table[:, inner] for outer in range(4) for inner in range(4)], axis=0
    )
    normal_matrix = jnp.dot(
        products,
        importance_factor,
        precision=lax.Precision.HIGHEST,
        preferred_element_type=jnp.float32,
    )
    right_side = jnp.dot(
        table.T,
        importance_factor * celestial_image,
        precision=lax.Precision.HIGHEST,
        preferred_element_type=jnp.float32,
    )
    coefficients = solve_cubic(normal_matrix, right_side)
    continuum = jnp.dot(
        table, coefficients, precision=lax.Precision.HIGHEST, preferred_element_type=jnp.float32
    )
    residual = celestial_image - continuum
    padded = jnp.pad(residual, ((1, 1), (0, 0)))
    smoothed = 0.25 * padded[:-2] + 0.5 * residual + 0.25 * padded[2:]
    return smoothed.reshape(channels, rows, columns)


def exact_onehot_dot(spec, first, second, data_first):
    data = first if data_first else second
    wide = lax.reduce_precision(data, exponent_bits=8, mantissa_bits=15)
    rest = data - wide
    parts = []
    for piece, precision in ((wide, lax.Precision.HIGH), (rest, lax.Precision.DEFAULT)):
        operands = (piece, second) if data_first else (first, piece)
        parts.append(
            jnp.einsum(spec, *operands, precision=precision, preferred_element_type=jnp.float32)
        )
    return parts[0] + parts[1]


def local(images, beam_weight, offsets, rejected_indicator, regression_indicator):
    ch_dev = images.shape[0]
    side = images.shape[2]
    all_channels = regression_indicator.shape[0]
    first_channel = lax.axis_index("chan") * ch_dev
    channel_ids = first_channel + jnp.arange(ch_dev, dtype=jnp.int32)
    exponent = 1.0 + 0.5 * channel_ids.astype(jnp.float32) / (all_channels - 1)
    log_weight = jnp.log(beam_weight)
    response = jnp.exp(exponent[:, None, None, None] * log_weight[None])
    stacked = jnp.stack([response * images, response * response])
    row_start = jnp.clip(offsets[:, 0], 0, MOS_ROWS - side)
    col_start = jnp.clip(offsets[:, 1], 0, MOS_COLS - side)
    row_hit = (
        lax.broadcasted_iota(jnp.int32, (1, MOS_ROWS, side), 1)
        == lax.broadcasted_iota(jnp.int32, (1, MOS_ROWS, side), 2) + row_start[:, None, None]
    ).astype(jnp.float32)
    col_hit = (
        lax.broadcasted_iota(jnp.int32, (1, side, MOS_COLS), 2)
        == lax.broadcasted_iota(jnp.int32, (1, side, MOS_COLS), 1) + col_start[:, None, None]
    ).astype(jnp.float32)
    rows_placed = exact_onehot_dot("bri,acbij->bacrj", row_hit, stacked, data_first=False)
    blocks = lax.psum(1, "beam")
    col_hit = col_hit.reshape(col_hit.shape[0], side, blocks, MOS_COLS // blocks)
    planes = jnp.einsum(
        "bacrj,bjnk->nacrk", rows_placed, col_hit, precision=lax.Precision.HIGHEST,
        preferred_element_type=jnp.float32,
    )
    own = lax.psum_scatter(planes, "beam", scatter_dimension=0, tiled=False)
    dividend_accumulator = own[0]
    normalizer_accumulated = own[1]
    accepted_entries = 1.0 - rejected_indicator.astype(jnp.float32)
    emission_absent = lax.dynamic_slice_in_dim(regression_indicator, first_channel, ch_dev).astype(
        jnp.float32
    )
    celestial_image = accepted_entries * dividend_accumulator / normalizer_accumulated
    importance_factor = normalizer_accumulated * (
        emission_absent[:, None, None] * accepted_entries + 0.01
    )
    arrived = lax.all_to_all(
        jnp.stack([celestial_image, importance_factor]), "chan", split_axis=2, concat_axis=1, tiled=True
    )
    return clean_pair((arrived[0], arrived[1]))


def solution(mesh):
    in_specs = (
        P("chan", "beam", None, None),
        P("beam", None, None),
        P("beam", None),
        P("chan", None, "beam"),
        P(),
    )
    out_specs = P(None, "chan", "beam")
    return jax.shard_map(local, mesh=mesh, in_specs=in_specs, out_specs=out_specs, check_vma=False)
```
